512 devices in a mesh: group: 4 (over z_hi), shard: 16 (over z_lo, y), tensor: 8 (over x, core).
Axes of the slice: x: 4, y: 4, z: 16 (z_hi: 4, z_lo: 4; z = z_hi * 4 + z_lo), core: 2. Of those that a mesh axis runs over, the one named last changes fastest.
Arguments:
- layer_delta: bfloat16 [4, 2, 4, 224, 4864], P('group', None, None, 'shard', 'tensor'), may hold values from -6 to 6
- emb_left: bfloat16 [4, 4, 19200, 64], P('group', None, ('shard', 'tensor')), may hold values from -6 to 6
- emb_right: bfloat16 [4, 64, 896], P('group'), may hold values from -0.75 to 0.75
- layer_weight: float32 [2, 896, 4864], P(None, ('group', 'shard'), 'tensor'), may hold values from -6 to 6
- layer_momentum: float32 [2, 896, 4864], P(None, ('group', 'shard'), 'tensor'), may hold values from -4 to 4
- emb_weight: float32 [76800, 896], P(('group', 'shard', 'tensor')), may hold values from -6 to 6
- emb_momentum: float32 [76800, 896], P(('group', 'shard', 'tensor')), may hold values from -4 to 4
Outputs:
- new_layer_weight: float32 [2, 896, 4864], P(None, ('group', 'shard'), 'tensor')
- new_layer_momentum: float32 [2, 896, 4864], P(None, ('group', 'shard'), 'tensor')
- layer_blocks: bfloat16 [2, 896, 4864], P(None, None, 'tensor')
- new_emb_weight: float32 [76800, 896], P(('group', 'shard', 'tensor'))
- new_emb_momentum: float32 [76800, 896], P(('group', 'shard', 'tensor'))
The draws below stay inside these ranges and needn't reach their ends.
All inputs are finite; a program needn't handle non-finite values.
Results may differ from the reference program's by a relative error of at most 0.0095.
Values may be sent and summed in bfloat16 or wider, within the bound.
No kernel may reach another device: no remote copies, remote signals or barrier semaphores. Data moves between devices by JAX's collectives and lax.ppermute only.
A program may use at most 64 MiB of HBM per device.

```python
import jax
import jax.numpy as jnp
from jax import lax

D = 896
FF = 4864
VOCAB = 76800
RANK = 64
N_GROUP = 4


def levels(own_key, extent, split, low, top_value):
    level = 1.0
    for dim, parts in split:
        heights = jax.random.uniform(jax.random.fold_in(jax.random.fold_in(own_key, 6), dim), (parts,), jnp.float32, low / len(split), top_value / len(split))
        level = level * jnp.repeat(jnp.exp(heights), extent[dim] // parts).reshape((-1,) + (1,) * (len(extent) - 1 - dim))
    return level


def centred(key, dims, spread, most, cuts=(), dtype=jnp.bfloat16):
    result = spread * jax.random.normal(key, dims, jnp.float32)
    if cuts:
        result = result * levels(key, dims, cuts, -0.22, 0.18)
    return jnp.clip(result, -most, most).astype(dtype)


def setup_inputs(seed: int = 0) -> dict:
    key_of = jax.random.split(jax.random.key(seed), 8)
    return {
        "layer_delta": centred(key_of[0], (N_GROUP, 2, N_GROUP, D // N_GROUP, FF), 1.0, 6.0, ((0, 4), (3, 16), (4, 8))),
        "emb_left": centred(key_of[1], (N_GROUP, N_GROUP, VOCAB // N_GROUP, RANK), 1.0, 6.0, ((0, 4), (2, 128))),
        "emb_right": centred(key_of[2], (N_GROUP, RANK, D), RANK ** -0.5, 0.75, ((0, 4),)),
        "layer_weight": centred(key_of[3], (2, D, FF), 1.0, 6.0, ((1, 64), (2, 8)), jnp.float32),
        "layer_momentum": centred(key_of[4], (2, D, FF), 0.5, 4.0, ((1, 64), (2, 8)), jnp.float32),
        "emb_weight": centred(key_of[5], (VOCAB, D), 1.0, 6.0, ((0, 512),), jnp.float32),
        "emb_momentum": centred(key_of[6], (VOCAB, D), 0.5, 4.0, ((0, 512),), jnp.float32),
    }


rate_outer = 0.7
beta_outer = 0.9


def reference(layer_delta, emb_left, emb_right, layer_weight, layer_momentum, emb_weight, emb_momentum):
    groups = layer_delta.shape[0]
    summed = jnp.sum(layer_delta.astype(jnp.float32), axis=0)
    layer_mean = summed.reshape(layer_weight.shape) / groups
    new_layer_momentum = beta_outer * layer_momentum + layer_mean
    new_layer_weight = layer_weight - rate_outer * (layer_mean + beta_outer * new_layer_momentum)
    layer_blocks = new_layer_weight.astype(jnp.bfloat16)

    def add_group(total, pair):
        left_part, right_part = pair
        rows = left_part.reshape(-1, left_part.shape[-1])
        product = jnp.dot(rows, right_part, preferred_element_type=jnp.float32).astype(jnp.bfloat16)
        return total + product.astype(jnp.float32), None

    start = jnp.zeros(emb_weight.shape, jnp.float32)
    total, unused = lax.scan(add_group, start, (emb_left, emb_right))
    emb_mean = total / groups
    new_emb_momentum = beta_outer * emb_momentum + emb_mean
    new_emb_weight = emb_weight - rate_outer * (emb_mean + beta_outer * new_emb_momentum)
    return (new_layer_weight, new_layer_momentum, layer_blocks, new_emb_weight, new_emb_momentum)
```

```python
import jax
import jax.numpy as jnp
from jax import lax
from jax.sharding import PartitionSpec as P

rate_outer = 0.7
beta_outer = 0.9

Y_SIZE = 4


def shift_pairs(n, k):
    return [(i, (i + k) % n) for i in range(n)]


def on_device(
    layer_delta, emb_left, emb_right, layer_weight, layer_momentum, emb_weight, emb_momentum
):
    f32 = jnp.float32
    groups = lax.axis_size("group")
    shards = lax.axis_size("shard")
    tensors = lax.axis_size("tensor")
    gi = lax.axis_index("group")
    si = lax.axis_index("shard")
    ti = lax.axis_index("tensor")

    delta = layer_delta[0]
    acc = lax.dynamic_index_in_dim(delta, gi, axis=1, keepdims=False).astype(f32)
    for k in range(1, groups):
        piece = lax.dynamic_index_in_dim(delta, (gi + k) % groups, axis=1, keepdims=False)
        acc = acc + lax.ppermute(piece, "group", shift_pairs(groups, k)).astype(f32)
    layer_mean = acc.reshape(layer_weight.shape) / groups
    new_layer_momentum = beta_outer * layer_momentum + layer_mean
    new_layer_weight = layer_weight - rate_outer * (layer_mean + beta_outer * new_layer_momentum)
    piece = new_layer_weight.astype(jnp.bfloat16)
    rows = piece.shape[1]

    yi = si % Y_SIZE
    ybase = si - yi
    yblk = jnp.zeros((piece.shape[0], Y_SIZE * rows, piece.shape[2]), piece.dtype)
    yblk = lax.dynamic_update_slice_in_dim(yblk, piece, yi * rows, axis=1)
    for k in range(1, Y_SIZE):
        pairs = [(s, (s - s % Y_SIZE) + (s % Y_SIZE + k) % Y_SIZE) for s in range(shards)]
        got = lax.ppermute(piece, "shard", pairs)
        yblk = lax.dynamic_update_slice_in_dim(yblk, got, ((yi - k) % Y_SIZE) * rows, axis=1)

    zlo_size = shards // Y_SIZE
    nz = groups * zlo_size
    zi = gi * zlo_size + si // Y_SIZE
    brows = Y_SIZE * rows
    n_all = groups * shards

    def zshift(k):
        pairs = []
        for idx in range(n_all):
            z, y = idx // Y_SIZE, idx % Y_SIZE
            pairs.append((idx, ((z + k) % nz) * Y_SIZE + y))
        return pairs

    out = jnp.zeros((piece.shape[0], nz * brows, piece.shape[2]), piece.dtype)
    out = lax.dynamic_update_slice_in_dim(out, yblk, zi * brows, axis=1)
    fwd = yblk
    bwd = yblk
    for step in range(1, nz // 2 + 1):
        fwd = lax.ppermute(fwd, ("group", "shard"), zshift(1))
        out = lax.dynamic_update_slice_in_dim(out, fwd, ((zi - step) % nz) * brows, axis=1)
        if step < nz - nz // 2:
            bwd = lax.ppermute(bwd, ("group", "shard"), zshift(-1))
            out = lax.dynamic_update_slice_in_dim(out, bwd, ((zi + step) % nz) * brows, axis=1)
    layer_blocks = out

    left = emb_left[0]
    right = emb_right[0]
    width = right.shape[1]
    chunk = width // tensors
    lefts = [None] * groups
    rights = [None] * groups
    lefts[0] = lax.dynamic_index_in_dim(left, gi, axis=0, keepdims=False)
    rchunk = lax.dynamic_slice_in_dim(right, ti * chunk, chunk, axis=1)
    rights[0] = rchunk
    for k in range(1, groups):
        lp = lax.dynamic_index_in_dim(left, (gi + k) % groups, axis=0, keepdims=False)
        lefts[k] = lax.ppermute(lp, "group", shift_pairs(groups, k))
        rights[k] = lax.ppermute(rchunk, "group", shift_pairs(groups, k))
    rstack = jnp.stack(rights, axis=0)
    full = jnp.zeros((groups, right.shape[0], width), right.dtype)
    full = lax.dynamic_update_slice_in_dim(full, rstack, ti * chunk, axis=2)
    for k in range(1, tensors):
        got = lax.ppermute(rstack, "tensor", shift_pairs(tensors, k))
        full = lax.dynamic_update_slice_in_dim(full, got, ((ti - k) % tensors) * chunk, axis=2)
    total = jnp.zeros(emb_weight.shape, f32)
    for k in range(groups):
        product = jnp.dot(lefts[k], full[k], preferred_element_type=f32).astype(jnp.bfloat16)
        total = total + product.astype(f32)
    emb_mean = total / groups
    new_emb_momentum = beta_outer * emb_momentum + emb_mean
    new_emb_weight = emb_weight - rate_outer * (emb_mean + beta_outer * new_emb_momentum)
    return (new_layer_weight, new_layer_momentum, layer_blocks, new_emb_weight, new_emb_momentum)


def solution(mesh):
    placed = (
        P("group", None, None, "shard", "tensor"),
        P("group", None, ("shard", "tensor"), None),
        P("group", None, None),
        P(None, ("group", "shard"), "tensor"),
        P(None, ("group", "shard"), "tensor"),
        P(("group", "shard", "tensor"), None),
        P(("group", "shard", "tensor"), None),
    )
    return jax.shard_map(
        on_device,
        mesh=mesh,
        in_specs=placed,
        out_specs=(
            P(None, ("group", "shard"), "tensor"),
            P(None, ("group", "shard"), "tensor"),
            P(None, None, "tensor"),
            P(("group", "shard", "tensor"), None),
            P(("group", "shard", "tensor"), None),
        ),
        check_vma=False,
    )
```

```python
import jax
import jax.numpy as jnp
from jax import lax
from jax.sharding import PartitionSpec as P

rate_outer = 0.7
beta_outer = 0.9

Y_SIZE = 4


def shift_pairs(n, k):
    return [(i, (i + k) % n) for i in range(n)]


def on_device(
    layer_delta, emb_left, emb_right, layer_weight, layer_momentum, emb_weight, emb_momentum
):
    f32 = jnp.float32
    bf16 = jnp.bfloat16
    groups = lax.axis_size("group")
    shards = lax.axis_size("shard")
    tensors = lax.axis_size("tensor")
    gi = lax.axis_index("group")
    si = lax.axis_index("shard")
    ti = lax.axis_index("tensor")

    delta = layer_delta[0]
    nlayer = delta.size // groups
    send_layer = jnp.moveaxis(delta, 1, 0).reshape(groups, nlayer)
    left = emb_left[0]
    nleft = left.size // groups
    send_left = left.reshape(groups, nleft)
    right = emb_right[0]
    rank, width = right.shape
    chunk = width // tensors
    rchunk = lax.dynamic_slice_in_dim(right, ti * chunk, chunk, axis=1)
    send_right = jnp.broadcast_to(rchunk.reshape(1, rank * chunk), (groups, rank * chunk))
    send = jnp.concatenate([send_layer, send_left, send_right], axis=1)
    recv = lax.all_to_all(send, "group", 0, 0, tiled=True)

    acc = recv[:, :nlayer].astype(f32).sum(axis=0)
    layer_mean = acc.reshape(layer_weight.shape) / groups
    new_layer_momentum = beta_outer * layer_momentum + layer_mean
    new_layer_weight = layer_weight - rate_outer * (layer_mean + beta_outer * new_layer_momentum)
    piece = new_layer_weight.astype(bf16)

    yi = si % Y_SIZE
    yblk = jnp.zeros((Y_SIZE,) + piece.shape, piece.dtype)
    yblk = lax.dynamic_update_index_in_dim(yblk, piece, yi, axis=0)
    for k in range(1, Y_SIZE):
        pairs = [(s, (s - s % Y_SIZE) + (s % Y_SIZE + k) % Y_SIZE) for s in range(shards)]
        got = lax.ppermute(piece, "shard", pairs)
        yblk = lax.dynamic_update_index_in_dim(yblk, got, (yi - k) % Y_SIZE, axis=0)

    zlo_size = shards // Y_SIZE
    nz = groups * zlo_size
    zi = gi * zlo_size + si // Y_SIZE
    n_all = groups * shards

    def zshift(k):
        return [(i, ((i // Y_SIZE + k) % nz) * Y_SIZE + i % Y_SIZE) for i in range(n_all)]

    out = jnp.zeros((nz,) + yblk.shape, piece.dtype)
    out = lax.dynamic_update_index_in_dim(out, yblk, zi, axis=0)
    fwd = yblk
    bwd = yblk
    for step in range(1, nz // 2 + 1):
        fwd = lax.ppermute(fwd, ("group", "shard"), zshift(1))
        out = lax.dynamic_update_index_in_dim(out, fwd, (zi - step) % nz, axis=0)
        if step < nz - nz // 2:
            bwd = lax.ppermute(bwd, ("group", "shard"), zshift(-1))
            out = lax.dynamic_update_index_in_dim(out, bwd, (zi + step) % nz, axis=0)
    layer_blocks = jnp.moveaxis(out, 2, 0).reshape(piece.shape[0], -1, piece.shape[2])

    lefts = recv[:, nlayer:nlayer + nleft].reshape((groups,) + left.shape[1:])
    rchunks = recv[:, nlayer + nleft:].reshape(groups, rank, chunk)
    rsend = jnp.broadcast_to(rchunks.reshape(1, -1), (tensors, rchunks.size))
    rgot = lax.all_to_all(rsend, "tensor", 0, 0, tiled=True)
    full = jnp.moveaxis(rgot.reshape(tensors, groups, rank, chunk), 0, 2).reshape(groups, rank, width)
    total = jnp.zeros(emb_weight.shape, f32)
    for g in range(groups):
        product = jnp.dot(lefts[g], full[g], preferred_element_type=f32).astype(bf16)
        total = total + product.astype(f32)
    emb_mean = total / groups
    new_emb_momentum = beta_outer * emb_momentum + emb_mean
    new_emb_weight = emb_weight - rate_outer * (emb_mean + beta_outer * new_emb_momentum)
    return (new_layer_weight, new_layer_momentum, layer_blocks, new_emb_weight, new_emb_momentum)


def solution(mesh):
    placed = (
        P("group", None, None, "shard", "tensor"),
        P("group", None, ("shard", "tensor"), None),
        P("group", None, None),
        P(None, ("group", "shard"), "tensor"),
        P(None, ("group", "shard"), "tensor"),
        P(("group", "shard", "tensor"), None),
        P(("group", "shard", "tensor"), None),
    )
    return jax.shard_map(
        on_device,
        mesh=mesh,
        in_specs=placed,
        out_specs=(
            P(None, ("group", "shard"), "tensor"),
            P(None, ("group", "shard"), "tensor"),
            P(None, None, "tensor"),
            P(("group", "shard", "tensor"), None),
            P(("group", "shard", "tensor"), None),
        ),
        check_vma=False,
    )
```

```python
import jax
import jax.numpy as jnp
from jax import lax
from jax.sharding import PartitionSpec as P

rate_outer = 0.7
beta_outer = 0.9

Y_SIZE = 4


def shift_pairs(n, k):
    return [(i, (i + k) % n) for i in range(n)]


def on_device(
    layer_delta, emb_left, emb_right, layer_weight, layer_momentum, emb_weight, emb_momentum
):
    f32 = jnp.float32
    bf16 = jnp.bfloat16
    groups = lax.axis_size("group")
    shards = lax.axis_size("shard")
    tensors = lax.axis_size("tensor")
    gi = lax.axis_index("group")
    si = lax.axis_index("shard")
    ti = lax.axis_index("tensor")

    delta = layer_delta[0]
    nlayer = delta.size // groups
    send_layer = jnp.moveaxis(delta, 1, 0).reshape(groups, nlayer)
    left = emb_left[0]
    nleft = left.size // groups
    send_left = left.reshape(groups, nleft)
    right = emb_right[0]
    rank, width = right.shape
    chunk = rank // tensors
    rchunk = lax.dynamic_slice_in_dim(right, ti * chunk, chunk, axis=0)
    send_right = jnp.broadcast_to(rchunk.reshape(1, chunk * width), (groups, chunk * width))
    send = jnp.concatenate([send_layer, send_left, send_right], axis=1)
    recv = lax.all_to_all(send, "group", 0, 0, tiled=True)

    acc = recv[:, :nlayer].astype(f32).sum(axis=0)
    layer_mean = acc.reshape(layer_weight.shape) / groups
    new_layer_momentum = beta_outer * layer_momentum + layer_mean
    new_layer_weight = layer_weight - rate_outer * (layer_mean + beta_outer * new_layer_momentum)
    piece = new_layer_weight.astype(bf16)

    yi = si % Y_SIZE
    yblk = jnp.zeros((Y_SIZE,) + piece.shape, piece.dtype)
    yblk = lax.dynamic_update_index_in_dim(yblk, piece, yi, axis=0)
    for k in range(1, Y_SIZE):
        pairs = [(s, (s - s % Y_SIZE) + (s % Y_SIZE + k) % Y_SIZE) for s in range(shards)]
        got = lax.ppermute(piece, "shard", pairs)
        yblk = lax.dynamic_update_index_in_dim(yblk, got, (yi - k) % Y_SIZE, axis=0)

    zlo_size = shards // Y_SIZE
    nz = groups * zlo_size
    zi = gi * zlo_size + si // Y_SIZE
    n_all = groups * shards

    def zshift(k):
        return [(i, ((i // Y_SIZE + k) % nz) * Y_SIZE + i % Y_SIZE) for i in range(n_all)]

    out = jnp.zeros((nz,) + yblk.shape, piece.dtype)
    out = lax.dynamic_update_index_in_dim(out, yblk, zi, axis=0)
    fwd = yblk
    bwd = yblk
    for step in range(1, nz // 2 + 1):
        fwd = lax.ppermute(fwd, ("group", "shard"), zshift(1))
        out = lax.dynamic_update_index_in_dim(out, fwd, (zi - step) % nz, axis=0)
        if step < nz - nz // 2:
            bwd = lax.ppermute(bwd, ("group", "shard"), zshift(-1))
            out = lax.dynamic_update_index_in_dim(out, bwd, (zi + step) % nz, axis=0)
    layer_blocks = jnp.moveaxis(out, 2, 0).reshape(piece.shape[0], -1, piece.shape[2])

    lefts = recv[:, nlayer:nlayer + nleft].reshape((groups,) + left.shape[1:])
    rchunks = recv[:, nlayer + nleft:].reshape(groups, chunk, width)
    full = lax.all_gather(rchunks, "tensor", axis=1, tiled=True)
    total = jnp.zeros(emb_weight.shape, f32)
    for g in range(groups):
        product = jnp.dot(lefts[g], full[g], preferred_element_type=f32).astype(bf16)
        total = total + product.astype(f32)
    emb_mean = total / groups
    new_emb_momentum = beta_outer * emb_momentum + emb_mean
    new_emb_weight = emb_weight - rate_outer * (emb_mean + beta_outer * new_emb_momentum)
    return (new_layer_weight, new_layer_momentum, layer_blocks, new_emb_weight, new_emb_momentum)


def solution(mesh):
    placed = (
        P("group", None, None, "shard", "tensor"),
        P("group", None, ("shard", "tensor"), None),
        P("group", None, None),
        P(None, ("group", "shard"), "tensor"),
        P(None, ("group", "shard"), "tensor"),
        P(("group", "shard", "tensor"), None),
        P(("group", "shard", "tensor"), None),
    )
    return jax.shard_map(
        on_device,
        mesh=mesh,
        in_specs=placed,
        out_specs=(
            P(None, ("group", "shard"), "tensor"),
            P(None, ("group", "shard"), "tensor"),
            P(None, None, "tensor"),
            P(("group", "shard", "tensor"), None),
            P(("group", "shard", "tensor"), None),
        ),
        check_vma=False,
    )
```

```python
import jax
import jax.numpy as jnp
from jax import lax
from jax.sharding import PartitionSpec as P

rate_outer = 0.7
beta_outer = 0.9

Y_SIZE = 4


def shift_pairs(n, k):
    return [(i, (i + k) % n) for i in range(n)]


def on_device(
    layer_delta, emb_left, emb_right, layer_weight, layer_momentum, emb_weight, emb_momentum
):
    f32 = jnp.float32
    bf16 = jnp.bfloat16
    groups = lax.axis_size("group")
    shards = lax.axis_size("shard")
    tensors = lax.axis_size("tensor")
    gi = lax.axis_index("group")
    si = lax.axis_index("shard")
    ti = lax.axis_index("tensor")

    delta = layer_delta[0]
    nlayer = delta.size // groups
    send_layer = jnp.moveaxis(delta, 1, 0).reshape(groups, nlayer)
    left = emb_left[0]
    nleft = left.size // groups
    send_left = left.reshape(groups, nleft)
    rights = lax.all_gather(emb_right, "group", axis=0, tiled=True)
    send = jnp.concatenate([send_layer, send_left], axis=1)
    recv = lax.all_to_all(send, "group", 0, 0, tiled=True)

    acc = recv[:, :nlayer].astype(f32).sum(axis=0)
    layer_mean = acc.reshape(layer_weight.shape) / groups
    new_layer_momentum = beta_outer * layer_momentum + layer_mean
    new_layer_weight = layer_weight - rate_outer * (layer_mean + beta_outer * new_layer_momentum)
    piece = new_layer_weight.astype(bf16)

    yi = si % Y_SIZE
    yblk = jnp.zeros((Y_SIZE,) + piece.shape, piece.dtype)
    yblk = lax.dynamic_update_index_in_dim(yblk, piece, yi, axis=0)
    for k in range(1, Y_SIZE):
        pairs = [(s, (s - s % Y_SIZE) + (s % Y_SIZE + k) % Y_SIZE) for s in range(shards)]
        got = lax.ppermute(piece, "shard", pairs)
        yblk = lax.dynamic_update_index_in_dim(yblk, got, (yi - k) % Y_SIZE, axis=0)

    zlo_size = shards // Y_SIZE
    nz = groups * zlo_size
    zi = gi * zlo_size + si // Y_SIZE
    n_all = groups * shards

    def zshift(k):
        return [(i, ((i // Y_SIZE + k) % nz) * Y_SIZE + i % Y_SIZE) for i in range(n_all)]

    out = jnp.zeros((nz,) + yblk.shape, piece.dtype)
    out = lax.dynamic_update_index_in_dim(out, yblk, zi, axis=0)
    fwd = yblk
    bwd = yblk
    for step in range(1, nz // 2 + 1):
        fwd = lax.ppermute(fwd, ("group", "shard"), zshift(1))
        out = lax.dynamic_update_index_in_dim(out, fwd, (zi - step) % nz, axis=0)
        if step < nz - nz // 2:
            bwd = lax.ppermute(bwd, ("group", "shard"), zshift(-1))
            out = lax.dynamic_update_index_in_dim(out, bwd, (zi + step) % nz, axis=0)
    layer_blocks = jnp.moveaxis(out, 2, 0).reshape(piece.shape[0], -1, piece.shape[2])

    lefts = recv[:, nlayer:nlayer + nleft].reshape((groups,) + left.shape[1:])
    total = jnp.zeros(emb_weight.shape, f32)
    for g in range(groups):
        product = jnp.dot(lefts[g], rights[g], preferred_element_type=f32).astype(bf16)
        total = total + product.astype(f32)
    emb_mean = total / groups
    new_emb_momentum = beta_outer * emb_momentum + emb_mean
    new_emb_weight = emb_weight - rate_outer * (emb_mean + beta_outer * new_emb_momentum)
    return (new_layer_weight, new_layer_momentum, layer_blocks, new_emb_weight, new_emb_momentum)


def solution(mesh):
    placed = (
        P("group", None, None, "shard", "tensor"),
        P("group", None, ("shard", "tensor"), None),
        P("group", None, None),
        P(None, ("group", "shard"), "tensor"),
        P(None, ("group", "shard"), "tensor"),
        P(("group", "shard", "tensor"), None),
        P(("group", "shard", "tensor"), None),
    )
    return jax.shard_map(
        on_device,
        mesh=mesh,
        in_specs=placed,
        out_specs=(
            P(None, ("group", "shard"), "tensor"),
            P(None, ("group", "shard"), "tensor"),
            P(None, None, "tensor"),
            P(("group", "shard", "tensor"), None),
            P(("group", "shard", "tensor"), None),
        ),
        check_vma=False,
    )
```

```python
import jax
import jax.numpy as jnp
from jax import lax
from jax.sharding import PartitionSpec as P

rate_outer = 0.7
beta_outer = 0.9

Y_SIZE = 4
OFFLOAD_MIN_BYTES = 1 << 20
LANES = 128


def shift_pairs(n, k):
    return [(i, (i + k) % n) for i in range(n)]


def on_device(
    layer_delta, emb_left, emb_right, layer_weight, layer_momentum, emb_weight, emb_momentum
):
    f32 = jnp.float32
    bf16 = jnp.bfloat16
    groups = lax.axis_size("group")
    shards = lax.axis_size("shard")
    tensors = lax.axis_size("tensor")
    gi = lax.axis_index("group")
    si = lax.axis_index("shard")
    ti = lax.axis_index("tensor")

    delta = layer_delta[0]
    nlayer = delta.size // groups
    send_layer = jnp.moveaxis(delta, 1, 0).reshape(groups, nlayer)
    left = emb_left[0]
    nleft = left.size // groups
    send_left = left.reshape(groups, nleft)
    right = emb_right[0]
    rank, width = right.shape
    chunk = rank // tensors
    rchunk = lax.dynamic_slice_in_dim(right, ti * chunk, chunk, axis=0)
    send_right = jnp.broadcast_to(rchunk.reshape(1, chunk * width), (groups, chunk * width))
    send = jnp.concatenate([send_layer, send_left, send_right], axis=1)
    recv = lax.all_to_all(send, "group", 0, 0, tiled=True)

    acc = recv[:, :nlayer].astype(f32).sum(axis=0)
    layer_mean = acc.reshape(layer_weight.shape) / groups
    new_layer_momentum = beta_outer * layer_momentum + layer_mean
    new_layer_weight = layer_weight - rate_outer * (layer_mean + beta_outer * new_layer_momentum)
    piece = new_layer_weight.astype(bf16)

    yi = si % Y_SIZE
    yblk = jnp.zeros((Y_SIZE,) + piece.shape, piece.dtype)
    yblk = lax.dynamic_update_index_in_dim(yblk, piece, yi, axis=0)
    for k in range(1, Y_SIZE):
        pairs = [(s, (s - s % Y_SIZE) + (s % Y_SIZE + k) % Y_SIZE) for s in range(shards)]
        got = lax.ppermute(piece, "shard", pairs)
        yblk = lax.dynamic_update_index_in_dim(yblk, got, (yi - k) % Y_SIZE, axis=0)

    zlo_size = shards // Y_SIZE
    nz = groups * zlo_size
    zi = gi * zlo_size + si // Y_SIZE
    n_all = groups * shards

    def zshift(k):
        return [(i, ((i // Y_SIZE + k) % nz) * Y_SIZE + i % Y_SIZE) for i in range(n_all)]

    out = jnp.zeros((nz,) + yblk.shape, piece.dtype)
    out = lax.dynamic_update_index_in_dim(out, yblk, zi, axis=0)
    fwd = yblk
    bwd = yblk
    for step in range(1, nz // 2 + 1):
        fwd = lax.ppermute(fwd, ("group", "shard"), zshift(1))
        out = lax.dynamic_update_index_in_dim(out, fwd, (zi - step) % nz, axis=0)
        if step < nz - nz // 2:
            bwd = lax.ppermute(bwd, ("group", "shard"), zshift(-1))
            out = lax.dynamic_update_index_in_dim(out, bwd, (zi + step) % nz, axis=0)
    layer_blocks = jnp.moveaxis(out, 2, 0).reshape(piece.shape[0], -1, piece.shape[2])

    lefts = recv[:, nlayer:nlayer + nleft].reshape((groups,) + left.shape[1:])
    rchunks = recv[:, nlayer + nleft:].reshape(groups, chunk, width)
    padded = -(-OFFLOAD_MIN_BYTES // (groups * rank * 2 * LANES)) * LANES
    rchunks = jnp.pad(rchunks, ((0, 0), (0, 0), (0, max(padded - width, 0))))
    rights = lax.all_gather(rchunks, "tensor", axis=1, tiled=True)[:, :, :width]
    total = jnp.zeros(emb_weight.shape, f32)
    for g in range(groups):
        product = jnp.dot(lefts[g], rights[g], preferred_element_type=f32).astype(bf16)
        total = total + product.astype(f32)
    emb_mean = total / groups
    new_emb_momentum = beta_outer * emb_momentum + emb_mean
    new_emb_weight = emb_weight - rate_outer * (emb_mean + beta_outer * new_emb_momentum)
    return (new_layer_weight, new_layer_momentum, layer_blocks, new_emb_weight, new_emb_momentum)


def solution(mesh):
    placed = (
        P("group", None, None, "shard", "tensor"),
        P("group", None, ("shard", "tensor"), None),
        P("group", None, None),
        P(None, ("group", "shard"), "tensor"),
        P(None, ("group", "shard"), "tensor"),
        P(("group", "shard", "tensor"), None),
        P(("group", "shard", "tensor"), None),
    )
    return jax.shard_map(
        on_device,
        mesh=mesh,
        in_specs=placed,
        out_specs=(
            P(None, ("group", "shard"), "tensor"),
            P(None, ("group", "shard"), "tensor"),
            P(None, None, "tensor"),
            P(("group", "shard", "tensor"), None),
            P(("group", "shard", "tensor"), None),
        ),
        check_vma=False,
    )
```

```python
import jax
import jax.numpy as jnp
from jax import lax
from jax.sharding import PartitionSpec as P

rate_outer = 0.7
beta_outer = 0.9

Y_SIZE = 4


def shift_pairs(n, k):
    return [(i, (i + k) % n) for i in range(n)]


def on_device(
    layer_delta, emb_left, emb_right, layer_weight, layer_momentum, emb_weight, emb_momentum
):
    f32 = jnp.float32
    bf16 = jnp.bfloat16
    groups = lax.axis_size("group")
    shards = lax.axis_size("shard")
    tensors = lax.axis_size("tensor")
    gi = lax.axis_index("group")
    si = lax.axis_index("shard")
    ti = lax.axis_index("tensor")

    delta = layer_delta[0]
    nlayer = delta.size // groups
    send_layer = jnp.moveaxis(delta, 1, 0).reshape(groups, nlayer)
    left = emb_left[0]
    nleft = left.size // groups
    send_left = left.reshape(groups, nleft)
    rights = lax.all_gather(emb_right, "group", axis=0, tiled=True)
    send = jnp.concatenate([send_layer, send_left], axis=1)
    recv = lax.all_to_all(send, "group", 0, 0, tiled=True)

    acc = recv[:, :nlayer].astype(f32).sum(axis=0)
    layer_mean = acc.reshape(layer_weight.shape) / groups
    new_layer_momentum = beta_outer * layer_momentum + layer_mean
    new_layer_weight = layer_weight - rate_outer * (layer_mean + beta_outer * new_layer_momentum)
    piece = new_layer_weight.astype(bf16)

    sgn = 1 - 2 * (ti % 2)
    n_st = shards * tensors

    def yshift(k):
        pairs = []
        for i in range(n_st):
            s, t = i // tensors, i % tensors
            d = k if t % 2 == 0 else -k
            pairs.append((i, ((s - s % Y_SIZE) + (s % Y_SIZE + d) % Y_SIZE) * tensors + t))
        return pairs

    yi = si % Y_SIZE
    yblk = jnp.zeros((Y_SIZE,) + piece.shape, piece.dtype)
    yblk = lax.dynamic_update_index_in_dim(yblk, piece, yi, axis=0)
    for k in (1, -1, 2):
        got = lax.ppermute(piece, ("shard", "tensor"), yshift(k))
        yblk = lax.dynamic_update_index_in_dim(yblk, got, (yi - k * sgn) % Y_SIZE, axis=0)

    zlo_size = shards // Y_SIZE
    nz = groups * zlo_size
    zi = gi * zlo_size + si // Y_SIZE
    n_all = groups * shards * tensors

    def zshift(k):
        pairs = []
        for i in range(n_all):
            gs, t = i // tensors, i % tensors
            z, y = gs // Y_SIZE, gs % Y_SIZE
            d = k if t % 2 == 0 else -k
            pairs.append((i, (((z + d) % nz) * Y_SIZE + y) * tensors + t))
        return pairs

    out = jnp.zeros((nz,) + yblk.shape, piece.dtype)
    out = lax.dynamic_update_index_in_dim(out, yblk, zi, axis=0)
    fwd = yblk
    bwd = yblk
    axes = ("group", "shard", "tensor")
    for step in range(1, nz // 2 + 1):
        fwd = lax.ppermute(fwd, axes, zshift(1))
        out = lax.dynamic_update_index_in_dim(out, fwd, (zi - step * sgn) % nz, axis=0)
        if step < nz - nz // 2:
            bwd = lax.ppermute(bwd, axes, zshift(-1))
            out = lax.dynamic_update_index_in_dim(out, bwd, (zi + step * sgn) % nz, axis=0)
    layer_blocks = jnp.moveaxis(out, 2, 0).reshape(piece.shape[0], -1, piece.shape[2])

    lefts = recv[:, nlayer:nlayer + nleft].reshape((groups,) + left.shape[1:])
    total = jnp.zeros(emb_weight.shape, f32)
    for g in range(groups):
        product = jnp.dot(lefts[g], rights[g], preferred_element_type=f32).astype(bf16)
        total = total + product.astype(f32)
    emb_mean = total / groups
    new_emb_momentum = beta_outer * emb_momentum + emb_mean
    new_emb_weight = emb_weight - rate_outer * (emb_mean + beta_outer * new_emb_momentum)
    return (new_layer_weight, new_layer_momentum, layer_blocks, new_emb_weight, new_emb_momentum)


def solution(mesh):
    placed = (
        P("group", None, None, "shard", "tensor"),
        P("group", None, ("shard", "tensor"), None),
        P("group", None, None),
        P(None, ("group", "shard"), "tensor"),
        P(None, ("group", "shard"), "tensor"),
        P(("group", "shard", "tensor"), None),
        P(("group", "shard", "tensor"), None),
    )
    return jax.shard_map(
        on_device,
        mesh=mesh,
        in_specs=placed,
        out_specs=(
            P(None, ("group", "shard"), "tensor"),
            P(None, ("group", "shard"), "tensor"),
            P(None, None, "tensor"),
            P(("group", "shard", "tensor"), None),
            P(("group", "shard", "tensor"), None),
        ),
        check_vma=False,
    )
```

```python
import jax
import jax.numpy as jnp
from jax import lax
from jax.sharding import PartitionSpec as P

rate_outer = 0.7
beta_outer = 0.9

Y_SIZE = 4


def shift_pairs(n, k):
    return [(i, (i + k) % n) for i in range(n)]


def on_device(
    layer_delta, emb_left, emb_right, layer_weight, layer_momentum, emb_weight, emb_momentum
):
    f32 = jnp.float32
    bf16 = jnp.bfloat16
    groups = lax.axis_size("group")
    shards = lax.axis_size("shard")
    tensors = lax.axis_size("tensor")
    gi = lax.axis_index("group")
    si = lax.axis_index("shard")
    ti = lax.axis_index("tensor")

    delta = layer_delta[0]
    nlayer = delta.size // groups
    send_layer = jnp.moveaxis(delta, 1, 0).reshape(groups, nlayer)
    left = emb_left[0]
    nleft = left.size // groups
    send_left = left.reshape(groups, nleft)
    right = emb_right[0]
    rank, width = right.shape
    rrows = rank // Y_SIZE
    ry = lax.dynamic_slice_in_dim(right, (si % Y_SIZE) * rrows, rrows, axis=0)
    send_right = jnp.broadcast_to(ry.reshape(1, rrows * width), (groups, rrows * width))
    send = jnp.concatenate([send_layer, send_left, send_right], axis=1)
    recv = lax.all_to_all(send, "group", 0, 0, tiled=True)

    acc = recv[:, :nlayer].astype(f32).sum(axis=0)
    layer_mean = acc.reshape(layer_weight.shape) / groups
    new_layer_momentum = beta_outer * layer_momentum + layer_mean
    new_layer_weight = layer_weight - rate_outer * (layer_mean + beta_outer * new_layer_momentum)
    piece = new_layer_weight.astype(bf16)

    sgn = 1 - 2 * (ti % 2)
    n_st = shards * tensors

    def yshift(k):
        pairs = []
        for i in range(n_st):
            s, t = i // tensors, i % tensors
            d = k if t % 2 == 0 else -k
            pairs.append((i, ((s - s % Y_SIZE) + (s % Y_SIZE + d) % Y_SIZE) * tensors + t))
        return pairs

    yi = si % Y_SIZE
    rgot = recv[:, nlayer + nleft:]
    npiece = piece.size
    payload = jnp.concatenate([piece.reshape(1, npiece), rgot.reshape(1, -1)], axis=1)
    yblk = jnp.zeros((Y_SIZE,) + piece.shape, piece.dtype)
    yblk = lax.dynamic_update_index_in_dim(yblk, piece, yi, axis=0)
    rights = jnp.zeros((groups, rank, width), rgot.dtype)
    rights = lax.dynamic_update_slice_in_dim(rights, rgot.reshape(groups, rrows, width), yi * rrows, axis=1)
    for k in (1, -1, 2):
        got = lax.ppermute(payload, ("shard", "tensor"), yshift(k))
        src = (yi - k * sgn) % Y_SIZE
        yblk = lax.dynamic_update_index_in_dim(yblk, got[0, :npiece].reshape(piece.shape), src, axis=0)
        rpart = got[0, npiece:].reshape(groups, rrows, width)
        rights = lax.dynamic_update_slice_in_dim(rights, rpart, src * rrows, axis=1)

    zlo_size = shards // Y_SIZE
    nz = groups * zlo_size
    zi = gi * zlo_size + si // Y_SIZE
    n_all = groups * shards * tensors

    def zshift(k):
        pairs = []
        for i in range(n_all):
            gs, t = i // tensors, i % tensors
            z, y = gs // Y_SIZE, gs % Y_SIZE
            d = k if t % 2 == 0 else -k
            pairs.append((i, (((z + d) % nz) * Y_SIZE + y) * tensors + t))
        return pairs

    out = jnp.zeros((nz,) + yblk.shape, piece.dtype)
    out = lax.dynamic_update_index_in_dim(out, yblk, zi, axis=0)
    fwd = yblk
    bwd = yblk
    axes = ("group", "shard", "tensor")
    for step in range(1, nz // 2 + 1):
        fwd = lax.ppermute(fwd, axes, zshift(1))
        out = lax.dynamic_update_index_in_dim(out, fwd, (zi - step * sgn) % nz, axis=0)
        if step < nz - nz // 2:
            bwd = lax.ppermute(bwd, axes, zshift(-1))
            out = lax.dynamic_update_index_in_dim(out, bwd, (zi + step * sgn) % nz, axis=0)
    layer_blocks = jnp.moveaxis(out, 2, 0).reshape(piece.shape[0], -1, piece.shape[2])

    lefts = recv[:, nlayer:nlayer + nleft].reshape((groups,) + left.shape[1:])
    total = jnp.zeros(emb_weight.shape, f32)
    for g in range(groups):
        product = jnp.dot(lefts[g], rights[g], preferred_element_type=f32).astype(bf16)
        total = total + product.astype(f32)
    emb_mean = total / groups
    new_emb_momentum = beta_outer * emb_momentum + emb_mean
    new_emb_weight = emb_weight - rate_outer * (emb_mean + beta_outer * new_emb_momentum)
    return (new_layer_weight, new_layer_momentum, layer_blocks, new_emb_weight, new_emb_momentum)


def solution(mesh):
    placed = (
        P("group", None, None, "shard", "tensor"),
        P("group", None, ("shard", "tensor"), None),
        P("group", None, None),
        P(None, ("group", "shard"), "tensor"),
        P(None, ("group", "shard"), "tensor"),
        P(("group", "shard", "tensor"), None),
        P(("group", "shard", "tensor"), None),
    )
    return jax.shard_map(
        on_device,
        mesh=mesh,
        in_specs=placed,
        out_specs=(
            P(None, ("group", "shard"), "tensor"),
            P(None, ("group", "shard"), "tensor"),
            P(None, None, "tensor"),
            P(("group", "shard", "tensor"), None),
            P(("group", "shard", "tensor"), None),
        ),
        check_vma=False,
    )
```

```python
import jax
import jax.numpy as jnp
from jax import lax
from jax.sharding import PartitionSpec as P

rate_outer = 0.7
beta_outer = 0.9

Y_SIZE = 4


def shift_pairs(n, k):
    return [(i, (i + k) % n) for i in range(n)]


def on_device(
    layer_delta, emb_left, emb_right, layer_weight, layer_momentum, emb_weight, emb_momentum
):
    f32 = jnp.float32
    bf16 = jnp.bfloat16
    groups = lax.axis_size("group")
    shards = lax.axis_size("shard")
    tensors = lax.axis_size("tensor")
    gi = lax.axis_index("group")
    si = lax.axis_index("shard")
    ti = lax.axis_index("tensor")

    delta = layer_delta[0]
    nlayer = delta.size // groups
    send_layer = jnp.moveaxis(delta, 1, 0).reshape(groups, nlayer)
    left = emb_left[0]
    nleft = left.size // groups
    send_left = left.reshape(groups, nleft)
    right = emb_right[0]
    rank, width = right.shape
    rrows = rank // Y_SIZE
    ry = lax.dynamic_slice_in_dim(right, (si % Y_SIZE) * rrows, rrows, axis=0)
    send_right = jnp.broadcast_to(ry.reshape(1, rrows * width), (groups, rrows * width))
    send = jnp.concatenate([send_layer, send_left, send_right], axis=1)
    recv = lax.all_to_all(send, "group", 0, 0, tiled=True)

    acc = recv[:, :nlayer].astype(f32).sum(axis=0)
    layer_mean = acc.reshape(layer_weight.shape) / groups
    new_layer_momentum = beta_outer * layer_momentum + layer_mean
    new_layer_weight = layer_weight - rate_outer * (layer_mean + beta_outer * new_layer_momentum)
    piece = new_layer_weight.astype(bf16)

    sgn = 1 - 2 * (ti % 2)
    n_st = shards * tensors

    def yshift(k):
        pairs = []
        for i in range(n_st):
            s, t = i // tensors, i % tensors
            d = k if t % 2 == 0 else -k
            pairs.append((i, ((s - s % Y_SIZE) + (s % Y_SIZE + d) % Y_SIZE) * tensors + t))
        return pairs

    yi = si % Y_SIZE
    rgot = recv[:, nlayer + nleft:]
    npiece = piece.size
    payload = jnp.concatenate([piece.reshape(1, npiece), rgot.reshape(1, -1)], axis=1)
    yblk = jnp.zeros((Y_SIZE,) + piece.shape, piece.dtype)
    yblk = lax.dynamic_update_index_in_dim(yblk, piece, yi, axis=0)
    rights = jnp.zeros((groups, rank, width), rgot.dtype)
    rights = lax.dynamic_update_slice_in_dim(rights, rgot.reshape(groups, rrows, width), yi * rrows, axis=1)
    for k in (1, -1, 2):
        got = lax.ppermute(payload, ("shard", "tensor"), yshift(k))
        src = (yi - k * sgn) % Y_SIZE
        yblk = lax.dynamic_update_index_in_dim(yblk, got[0, :npiece].reshape(piece.shape), src, axis=0)
        rpart = got[0, npiece:].reshape(groups, rrows, width)
        rights = lax.dynamic_update_slice_in_dim(rights, rpart, src * rrows, axis=1)

    zlo_size = shards // Y_SIZE
    nz = groups * zlo_size
    zi = gi * zlo_size + si // Y_SIZE
    n_all = groups * shards * tensors

    def zshift(k):
        pairs = []
        for i in range(n_all):
            gs, t = i // tensors, i % tensors
            z, y = gs // Y_SIZE, gs % Y_SIZE
            d = k if t % 2 == 0 else -k
            pairs.append((i, (((z + d) % nz) * Y_SIZE + y) * tensors + t))
        return pairs

    out = jnp.zeros((nz,) + yblk.shape, piece.dtype)
    out = lax.dynamic_update_index_in_dim(out, yblk, zi, axis=0)
    half = nz // 2
    reach = half // 2
    rel = jnp.zeros((2 * reach + 1,) + yblk.shape, piece.dtype)
    rel = lax.dynamic_update_index_in_dim(rel, yblk, reach, axis=0)
    fwd = yblk
    bwd = yblk
    axes = ("group", "shard", "tensor")
    for step in range(1, reach + 1):
        fwd = lax.ppermute(fwd, axes, zshift(2))
        j = -step * sgn
        out = lax.dynamic_update_index_in_dim(out, fwd, (zi + 2 * j) % nz, axis=0)
        rel = lax.dynamic_update_index_in_dim(rel, fwd, j + reach, axis=0)
        if step < half - reach:
            bwd = lax.ppermute(bwd, axes, zshift(-2))
            out = lax.dynamic_update_index_in_dim(out, bwd, (zi - 2 * j) % nz, axis=0)
            rel = lax.dynamic_update_index_in_dim(rel, bwd, reach - j, axis=0)
    nsend = reach
    up_start = reach
    down_start = reach - (nsend - 1)
    for k, first in ((-1, (up_start + down_start + (up_start - down_start) * sgn) // 2),
                     (1, (up_start + down_start - (up_start - down_start) * sgn) // 2)):
        part = lax.dynamic_slice_in_dim(rel, first, nsend, axis=0)
        got = lax.ppermute(part, axes, zshift(k))
        src_z = zi - k * sgn
        for m in range(nsend):
            zabs = (src_z + 2 * (first - reach + m)) % nz
            out = lax.dynamic_update_index_in_dim(out, got[m], zabs, axis=0)
    layer_blocks = jnp.moveaxis(out, 2, 0).reshape(piece.shape[0], -1, piece.shape[2])

    lefts = recv[:, nlayer:nlayer + nleft].reshape((groups,) + left.shape[1:])
    total = jnp.zeros(emb_weight.shape, f32)
    for g in range(groups):
        product = jnp.dot(lefts[g], rights[g], preferred_element_type=f32).astype(bf16)
        total = total + product.astype(f32)
    emb_mean = total / groups
    new_emb_momentum = beta_outer * emb_momentum + emb_mean
    new_emb_weight = emb_weight - rate_outer * (emb_mean + beta_outer * new_emb_momentum)
    return (new_layer_weight, new_layer_momentum, layer_blocks, new_emb_weight, new_emb_momentum)


def solution(mesh):
    placed = (
        P("group", None, None, "shard", "tensor"),
        P("group", None, ("shard", "tensor"), None),
        P("group", None, None),
        P(None, ("group", "shard"), "tensor"),
        P(None, ("group", "shard"), "tensor"),
        P(("group", "shard", "tensor"), None),
        P(("group", "shard", "tensor"), None),
    )
    return jax.shard_map(
        on_device,
        mesh=mesh,
        in_specs=placed,
        out_specs=(
            P(None, ("group", "shard"), "tensor"),
            P(None, ("group", "shard"), "tensor"),
            P(None, None, "tensor"),
            P(("group", "shard", "tensor"), None),
            P(("group", "shard", "tensor"), None),
        ),
        check_vma=False,
    )
```

```python
import jax
import jax.numpy as jnp
from jax import lax
from jax.sharding import PartitionSpec as P

rate_outer = 0.7
beta_outer = 0.9

Y_SIZE = 4


def shift_pairs(n, k):
    return [(i, (i + k) % n) for i in range(n)]


def on_device(
    layer_delta, emb_left, emb_right, layer_weight, layer_momentum, emb_weight, emb_momentum
):
    f32 = jnp.float32
    bf16 = jnp.bfloat16
    groups = lax.axis_size("group")
    shards = lax.axis_size("shard")
    tensors = lax.axis_size("tensor")
    gi = lax.axis_index("group")
    si = lax.axis_index("shard")
    ti = lax.axis_index("tensor")

    delta = layer_delta[0]
    nlayer = delta.size // groups
    send_layer = jnp.moveaxis(delta, 1, 0).reshape(groups, nlayer)
    left = emb_left[0]
    nleft = left.size // groups
    send_left = left.reshape(groups, nleft)
    right = emb_right[0]
    rank, width = right.shape
    send_right = jnp.broadcast_to(right.reshape(1, rank * width), (groups, rank * width))
    send = jnp.concatenate([send_layer, send_left, send_right], axis=1)
    recv = lax.all_to_all(send, "group", 0, 0, tiled=True)

    acc = recv[:, :nlayer].astype(f32).sum(axis=0)
    layer_mean = acc.reshape(layer_weight.shape) / groups
    new_layer_momentum = beta_outer * layer_momentum + layer_mean
    new_layer_weight = layer_weight - rate_outer * (layer_mean + beta_outer * new_layer_momentum)
    piece = new_layer_weight.astype(bf16)

    sgn = 1 - 2 * (ti % 2)
    n_st = shards * tensors

    def yshift(k):
        pairs = []
        for i in range(n_st):
            s, t = i // tensors, i % tensors
            d = k if t % 2 == 0 else -k
            pairs.append((i, ((s - s % Y_SIZE) + (s % Y_SIZE + d) % Y_SIZE) * tensors + t))
        return pairs

    axes = ("group", "shard", "tensor")
    zlo_size = shards // Y_SIZE
    nz = groups * zlo_size
    zi = gi * zlo_size + si // Y_SIZE
    n_all = groups * shards * tensors

    def zshift(k):
        pairs = []
        for i in range(n_all):
            gs, t = i // tensors, i % tensors
            z, y = gs // Y_SIZE, gs % Y_SIZE
            d = k if t % 2 == 0 else -k
            pairs.append((i, (((z + d) % nz) * Y_SIZE + y) * tensors + t))
        return pairs

    zblk = jnp.zeros((nz,) + piece.shape, piece.dtype)
    zblk = lax.dynamic_update_index_in_dim(zblk, piece, zi, axis=0)
    half = nz // 2
    reach = half // 2
    rel = jnp.zeros((2 * reach + 1,) + piece.shape, piece.dtype)
    rel = lax.dynamic_update_index_in_dim(rel, piece, reach, axis=0)
    fwd = piece
    bwd = piece
    for step in range(1, reach + 1):
        fwd = lax.ppermute(fwd, axes, zshift(2))
        j = -step * sgn
        zblk = lax.dynamic_update_index_in_dim(zblk, fwd, (zi + 2 * j) % nz, axis=0)
        rel = lax.dynamic_update_index_in_dim(rel, fwd, j + reach, axis=0)
        if step < half - reach:
            bwd = lax.ppermute(bwd, axes, zshift(-2))
            zblk = lax.dynamic_update_index_in_dim(zblk, bwd, (zi - 2 * j) % nz, axis=0)
            rel = lax.dynamic_update_index_in_dim(rel, bwd, reach - j, axis=0)
    nsend = reach
    up_start = reach
    down_start = reach - (nsend - 1)
    for k, first in ((-1, (up_start + down_start + (up_start - down_start) * sgn) // 2),
                     (1, (up_start + down_start - (up_start - down_start) * sgn) // 2)):
        part = lax.dynamic_slice_in_dim(rel, first, nsend, axis=0)
        got = lax.ppermute(part, axes, zshift(k))
        src_z = zi - k * sgn
        for m in range(nsend):
            zabs = (src_z + 2 * (first - reach + m)) % nz
            zblk = lax.dynamic_update_index_in_dim(zblk, got[m], zabs, axis=0)

    yi = si % Y_SIZE
    yout = jnp.zeros((Y_SIZE,) + zblk.shape, piece.dtype)
    yout = lax.dynamic_update_index_in_dim(yout, zblk, yi, axis=0)
    for k in (1, -1, 2):
        got = lax.ppermute(zblk, ("shard", "tensor"), yshift(k))
        yout = lax.dynamic_update_index_in_dim(yout, got, (yi - k * sgn) % Y_SIZE, axis=0)
    out = jnp.swapaxes(yout, 0, 1)
    layer_blocks = jnp.moveaxis(out, 2, 0).reshape(piece.shape[0], -1, piece.shape[2])

    lefts = recv[:, nlayer:nlayer + nleft].reshape((groups,) + left.shape[1:])
    rights = recv[:, nlayer + nleft:].reshape(groups, rank, width)
    total = jnp.zeros(emb_weight.shape, f32)
    for g in range(groups):
        product = jnp.dot(lefts[g], rights[g], preferred_element_type=f32).astype(bf16)
        total = total + product.astype(f32)
    emb_mean = total / groups
    new_emb_momentum = beta_outer * emb_momentum + emb_mean
    new_emb_weight = emb_weight - rate_outer * (emb_mean + beta_outer * new_emb_momentum)
    return (new_layer_weight, new_layer_momentum, layer_blocks, new_emb_weight, new_emb_momentum)


def solution(mesh):
    placed = (
        P("group", None, None, "shard", "tensor"),
        P("group", None, ("shard", "tensor"), None),
        P("group", None, None),
        P(None, ("group", "shard"), "tensor"),
        P(None, ("group", "shard"), "tensor"),
        P(("group", "shard", "tensor"), None),
        P(("group", "shard", "tensor"), None),
    )
    return jax.shard_map(
        on_device,
        mesh=mesh,
        in_specs=placed,
        out_specs=(
            P(None, ("group", "shard"), "tensor"),
            P(None, ("group", "shard"), "tensor"),
            P(None, None, "tensor"),
            P(("group", "shard", "tensor"), None),
            P(("group", "shard", "tensor"), None),
        ),
        check_vma=False,
    )
```

```python
import jax
import jax.numpy as jnp
from jax import lax
from jax.sharding import PartitionSpec as P

rate_outer = 0.7
beta_outer = 0.9

Y_SIZE = 4


def shift_pairs(n, k):
    return [(i, (i + k) % n) for i in range(n)]


def on_device(
    layer_delta, emb_left, emb_right, layer_weight, layer_momentum, emb_weight, emb_momentum
):
    f32 = jnp.float32
    bf16 = jnp.bfloat16
    groups = lax.axis_size("group")
    shards = lax.axis_size("shard")
    tensors = lax.axis_size("tensor")
    gi = lax.axis_index("group")
    si = lax.axis_index("shard")
    ti = lax.axis_index("tensor")

    delta = layer_delta[0]
    nlayer = delta.size // groups
    send_layer = jnp.moveaxis(delta, 1, 0).reshape(groups, nlayer)
    left = emb_left[0]
    nleft = left.size // groups
    send_left = left.reshape(groups, nleft)
    right = emb_right[0]
    rank, width = right.shape
    rrows = rank // Y_SIZE
    ry = lax.dynamic_slice_in_dim(right, (si % Y_SIZE) * rrows, rrows, axis=0)
    send_right = jnp.broadcast_to(ry.reshape(1, rrows * width), (groups, rrows * width))
    send = jnp.concatenate([send_layer, send_left, send_right], axis=1)
    recv = lax.all_to_all(send, "group", 0, 0, tiled=True)

    acc = recv[:, :nlayer].astype(f32).sum(axis=0)
    layer_mean = acc.reshape(layer_weight.shape) / groups
    new_layer_momentum = beta_outer * layer_momentum + layer_mean
    new_layer_weight = layer_weight - rate_outer * (layer_mean + beta_outer * new_layer_momentum)
    piece = new_layer_weight.astype(bf16)

    sgn = 1 - 2 * (ti % 2)
    n_st = shards * tensors

    def yshift(k):
        pairs = []
        for i in range(n_st):
            s, t = i // tensors, i % tensors
            d = k if t % 2 == 0 else -k
            pairs.append((i, ((s - s % Y_SIZE) + (s % Y_SIZE + d) % Y_SIZE) * tensors + t))
        return pairs

    yi = si % Y_SIZE
    rgot = recv[:, nlayer + nleft:]
    npiece = piece.size
    payload = jnp.concatenate([piece.reshape(1, npiece), rgot.reshape(1, -1)], axis=1)
    yblk = jnp.zeros((Y_SIZE,) + piece.shape, piece.dtype)
    yblk = lax.dynamic_update_index_in_dim(yblk, piece, yi, axis=0)
    rights = jnp.zeros((groups, rank, width), rgot.dtype)
    rights = lax.dynamic_update_slice_in_dim(rights, rgot.reshape(groups, rrows, width), yi * rrows, axis=1)
    for k in (1, -1, 2):
        got = lax.ppermute(payload, ("shard", "tensor"), yshift(k))
        src = (yi - k * sgn) % Y_SIZE
        yblk = lax.dynamic_update_index_in_dim(yblk, got[0, :npiece].reshape(piece.shape), src, axis=0)
        rpart = got[0, npiece:].reshape(groups, rrows, width)
        rights = lax.dynamic_update_slice_in_dim(rights, rpart, src * rrows, axis=1)

    zlo_size = shards // Y_SIZE
    nz = groups * zlo_size
    zi = gi * zlo_size + si // Y_SIZE
    n_all = groups * shards * tensors

    def zshift(k):
        pairs = []
        for i in range(n_all):
            gs, t = i // tensors, i % tensors
            z, y = gs // Y_SIZE, gs % Y_SIZE
            d = k if t % 2 == 0 else -k
            pairs.append((i, (((z + d) % nz) * Y_SIZE + y) * tensors + t))
        return pairs

    out = jnp.zeros((nz,) + yblk.shape, piece.dtype)
    out = lax.dynamic_update_index_in_dim(out, yblk, zi, axis=0)
    half = nz // 2
    reach = half // 2
    rel = jnp.zeros((2 * reach + 1,) + yblk.shape, piece.dtype)
    rel = lax.dynamic_update_index_in_dim(rel, yblk, reach, axis=0)
    fwd = yblk
    bwd = yblk
    axes = ("group", "shard", "tensor")
    for step in range(1, reach + 1):
        fwd = lax.ppermute(fwd, axes, zshift(2))
        j = -step * sgn
        out = lax.dynamic_update_index_in_dim(out, fwd, (zi + 2 * j) % nz, axis=0)
        if step < reach:
            rel = lax.dynamic_update_index_in_dim(rel, fwd, j + reach, axis=0)
        if step < half - reach:
            bwd = lax.ppermute(bwd, axes, zshift(-2))
            out = lax.dynamic_update_index_in_dim(out, bwd, (zi - 2 * j) % nz, axis=0)
            rel = lax.dynamic_update_index_in_dim(rel, bwd, reach - j, axis=0)
    nsend = reach
    up_start = reach
    down_start = reach - (nsend - 1)
    for k, first in ((-1, (up_start + down_start + (up_start - down_start) * sgn) // 2),
                     (1, (up_start + down_start - (up_start - down_start) * sgn) // 2)):
        part = lax.dynamic_slice_in_dim(rel, first, nsend, axis=0)
        got = lax.ppermute(part, axes, zshift(k))
        src_z = zi - k * sgn
        for m in range(nsend):
            zabs = (src_z + 2 * (first - reach + m)) % nz
            out = lax.dynamic_update_index_in_dim(out, got[m], zabs, axis=0)
    layer_blocks = jnp.moveaxis(out, 2, 0).reshape(piece.shape[0], -1, piece.shape[2])

    lefts = recv[:, nlayer:nlayer + nleft].reshape((groups,) + left.shape[1:])
    total = jnp.zeros(emb_weight.shape, f32)
    for g in range(groups):
        product = jnp.dot(lefts[g], rights[g], preferred_element_type=f32).astype(bf16)
        total = total + product.astype(f32)
    emb_mean = total / groups
    new_emb_momentum = beta_outer * emb_momentum + emb_mean
    new_emb_weight = emb_weight - rate_outer * (emb_mean + beta_outer * new_emb_momentum)
    return (new_layer_weight, new_layer_momentum, layer_blocks, new_emb_weight, new_emb_momentum)


def solution(mesh):
    placed = (
        P("group", None, None, "shard", "tensor"),
        P("group", None, ("shard", "tensor"), None),
        P("group", None, None),
        P(None, ("group", "shard"), "tensor"),
        P(None, ("group", "shard"), "tensor"),
        P(("group", "shard", "tensor"), None),
        P(("group", "shard", "tensor"), None),
    )
    return jax.shard_map(
        on_device,
        mesh=mesh,
        in_specs=placed,
        out_specs=(
            P(None, ("group", "shard"), "tensor"),
            P(None, ("group", "shard"), "tensor"),
            P(None, None, "tensor"),
            P(("group", "shard", "tensor"), None),
            P(("group", "shard", "tensor"), None),
        ),
        check_vma=False,
    )
```

```python
import jax
import jax.numpy as jnp
from jax import lax
from jax.sharding import PartitionSpec as P

rate_outer = 0.7
beta_outer = 0.9

Y_SIZE = 4


def shift_pairs(n, k):
    return [(i, (i + k) % n) for i in range(n)]


def on_device(
    layer_delta, emb_left, emb_right, layer_weight, layer_momentum, emb_weight, emb_momentum
):
    f32 = jnp.float32
    bf16 = jnp.bfloat16
    groups = lax.axis_size("group")
    shards = lax.axis_size("shard")
    tensors = lax.axis_size("tensor")
    gi = lax.axis_index("group")
    si = lax.axis_index("shard")
    ti = lax.axis_index("tensor")

    delta = layer_delta[0]
    nlayer = delta.size // groups
    send_layer = jnp.moveaxis(delta, 1, 0).reshape(groups, nlayer)
    left = emb_left[0]
    nleft = left.size // groups
    send_left = left.reshape(groups, nleft)
    right = emb_right[0]
    rank, width = right.shape
    rrows = rank // Y_SIZE
    ry = lax.dynamic_slice_in_dim(right, (si % Y_SIZE) * rrows, rrows, axis=0)
    send_right = jnp.broadcast_to(ry.reshape(1, rrows * width), (groups, rrows * width))
    send = jnp.concatenate([send_layer, send_left, send_right], axis=1)
    recv = lax.all_to_all(send, "group", 0, 0, tiled=True)

    acc = recv[:, :nlayer].astype(f32).sum(axis=0)
    layer_mean = acc.reshape(layer_weight.shape) / groups
    new_layer_momentum = beta_outer * layer_momentum + layer_mean
    new_layer_weight = layer_weight - rate_outer * (layer_mean + beta_outer * new_layer_momentum)
    piece = new_layer_weight.astype(bf16)

    sgn = 1
    n_st = shards * tensors

    def yshift(k):
        pairs = []
        for i in range(n_st):
            s, t = i // tensors, i % tensors
            d = k
            pairs.append((i, ((s - s % Y_SIZE) + (s % Y_SIZE + d) % Y_SIZE) * tensors + t))
        return pairs

    yi = si % Y_SIZE
    rgot = recv[:, nlayer + nleft:]
    npiece = piece.size
    payload = jnp.concatenate([piece.reshape(1, npiece), rgot.reshape(1, -1)], axis=1)
    yblk = jnp.zeros((Y_SIZE,) + piece.shape, piece.dtype)
    yblk = lax.dynamic_update_index_in_dim(yblk, piece, yi, axis=0)
    rights = jnp.zeros((groups, rank, width), rgot.dtype)
    rights = lax.dynamic_update_slice_in_dim(rights, rgot.reshape(groups, rrows, width), yi * rrows, axis=1)
    for k in (1, -1, 2):
        got = lax.ppermute(payload, ("shard", "tensor"), yshift(k))
        src = (yi - k * sgn) % Y_SIZE
        yblk = lax.dynamic_update_index_in_dim(yblk, got[0, :npiece].reshape(piece.shape), src, axis=0)
        rpart = got[0, npiece:].reshape(groups, rrows, width)
        rights = lax.dynamic_update_slice_in_dim(rights, rpart, src * rrows, axis=1)

    zlo_size = shards // Y_SIZE
    nz = groups * zlo_size
    zi = gi * zlo_size + si // Y_SIZE
    n_all = groups * shards * tensors

    def zshift(k):
        pairs = []
        for i in range(n_all):
            gs, t = i // tensors, i % tensors
            z, y = gs // Y_SIZE, gs % Y_SIZE
            d = k
            pairs.append((i, (((z + d) % nz) * Y_SIZE + y) * tensors + t))
        return pairs

    out = jnp.zeros((nz,) + yblk.shape, piece.dtype)
    out = lax.dynamic_update_index_in_dim(out, yblk, zi, axis=0)
    half = nz // 2
    reach = half // 2
    rel = jnp.zeros((2 * reach + 1,) + yblk.shape, piece.dtype)
    rel = lax.dynamic_update_index_in_dim(rel, yblk, reach, axis=0)
    fwd = yblk
    bwd = yblk
    axes = ("group", "shard", "tensor")
    for step in range(1, reach + 1):
        fwd = lax.ppermute(fwd, axes, zshift(2))
        j = -step * sgn
        out = lax.dynamic_update_index_in_dim(out, fwd, (zi + 2 * j) % nz, axis=0)
        if step < reach:
            rel = lax.dynamic_update_index_in_dim(rel, fwd, j + reach, axis=0)
        if step < half - reach:
            bwd = lax.ppermute(bwd, axes, zshift(-2))
            out = lax.dynamic_update_index_in_dim(out, bwd, (zi - 2 * j) % nz, axis=0)
            rel = lax.dynamic_update_index_in_dim(rel, bwd, reach - j, axis=0)
    nsend = reach
    up_start = reach
    down_start = reach - (nsend - 1)
    for k, first in ((-1, (up_start + down_start + (up_start - down_start) * sgn) // 2),
                     (1, (up_start + down_start - (up_start - down_start) * sgn) // 2)):
        part = lax.dynamic_slice_in_dim(rel, first, nsend, axis=0)
        got = lax.ppermute(part, axes, zshift(k))
        src_z = zi - k * sgn
        for m in range(nsend):
            zabs = (src_z + 2 * (first - reach + m)) % nz
            out = lax.dynamic_update_index_in_dim(out, got[m], zabs, axis=0)
    layer_blocks = jnp.moveaxis(out, 2, 0).reshape(piece.shape[0], -1, piece.shape[2])

    lefts = recv[:, nlayer:nlayer + nleft].reshape((groups,) + left.shape[1:])
    total = jnp.zeros(emb_weight.shape, f32)
    for g in range(groups):
        product = jnp.dot(lefts[g], rights[g], preferred_element_type=f32).astype(bf16)
        total = total + product.astype(f32)
    emb_mean = total / groups
    new_emb_momentum = beta_outer * emb_momentum + emb_mean
    new_emb_weight = emb_weight - rate_outer * (emb_mean + beta_outer * new_emb_momentum)
    return (new_layer_weight, new_layer_momentum, layer_blocks, new_emb_weight, new_emb_momentum)


def solution(mesh):
    placed = (
        P("group", None, None, "shard", "tensor"),
        P("group", None, ("shard", "tensor"), None),
        P("group", None, None),
        P(None, ("group", "shard"), "tensor"),
        P(None, ("group", "shard"), "tensor"),
        P(("group", "shard", "tensor"), None),
        P(("group", "shard", "tensor"), None),
    )
    return jax.shard_map(
        on_device,
        mesh=mesh,
        in_specs=placed,
        out_specs=(
            P(None, ("group", "shard"), "tensor"),
            P(None, ("group", "shard"), "tensor"),
            P(None, None, "tensor"),
            P(("group", "shard", "tensor"), None),
            P(("group", "shard", "tensor"), None),
        ),
        check_vma=False,
    )
```

```python
import jax
import jax.numpy as jnp
from jax import lax
from jax.sharding import PartitionSpec as P

rate_outer = 0.7
beta_outer = 0.9

Y_SIZE = 4


def shift_pairs(n, k):
    return [(i, (i + k) % n) for i in range(n)]


def on_device(
    layer_delta, emb_left, emb_right, layer_weight, layer_momentum, emb_weight, emb_momentum
):
    f32 = jnp.float32
    bf16 = jnp.bfloat16
    groups = lax.axis_size("group")
    shards = lax.axis_size("shard")
    tensors = lax.axis_size("tensor")
    gi = lax.axis_index("group")
    si = lax.axis_index("shard")
    ti = lax.axis_index("tensor")

    delta = layer_delta[0]
    nlayer = delta.size // groups
    send_layer = jnp.moveaxis(delta, 1, 0).reshape(groups, nlayer)
    left = emb_left[0]
    nleft = left.size // groups
    send_left = left.reshape(groups, nleft)
    right = emb_right[0]
    rank, width = right.shape
    rrows = rank // Y_SIZE
    ry = lax.dynamic_slice_in_dim(right, (si % Y_SIZE) * rrows, rrows, axis=0)
    send_right = jnp.broadcast_to(ry.reshape(1, rrows * width), (groups, rrows * width))
    parts = [send_layer, send_left, send_right]
    send = jnp.concatenate([p.reshape(groups, 2, p.shape[1] // 2) for p in parts], axis=2)
    recv_halves = lax.all_to_all(send, "group", 0, 0, tiled=True)

    def received(offset, n):
        return recv_halves[:, :, offset // 2:(offset + n) // 2].reshape(groups, n)

    acc = received(0, nlayer).astype(f32).sum(axis=0)
    layer_mean = acc.reshape(layer_weight.shape) / groups
    new_layer_momentum = beta_outer * layer_momentum + layer_mean
    new_layer_weight = layer_weight - rate_outer * (layer_mean + beta_outer * new_layer_momentum)
    piece = new_layer_weight.astype(bf16)

    sgn = 1 - 2 * (ti % 2)
    n_st = shards * tensors

    def yshift(k):
        pairs = []
        for i in range(n_st):
            s, t = i // tensors, i % tensors
            d = k if t % 2 == 0 else -k
            pairs.append((i, ((s - s % Y_SIZE) + (s % Y_SIZE + d) % Y_SIZE) * tensors + t))
        return pairs

    yi = si % Y_SIZE
    rgot = received(nlayer + nleft, rrows * width)
    npiece = piece.size
    payload = jnp.concatenate([piece.reshape(1, npiece), rgot.reshape(1, -1)], axis=1)
    yblk = jnp.zeros((Y_SIZE,) + piece.shape, piece.dtype)
    yblk = lax.dynamic_update_index_in_dim(yblk, piece, yi, axis=0)
    rights = jnp.zeros((groups, rank, width), rgot.dtype)
    rights = lax.dynamic_update_slice_in_dim(rights, rgot.reshape(groups, rrows, width), yi * rrows, axis=1)
    for k in (1, -1, 2):
        got = lax.ppermute(payload, ("shard", "tensor"), yshift(k))
        src = (yi - k * sgn) % Y_SIZE
        yblk = lax.dynamic_update_index_in_dim(yblk, got[0, :npiece].reshape(piece.shape), src, axis=0)
        rpart = got[0, npiece:].reshape(groups, rrows, width)
        rights = lax.dynamic_update_slice_in_dim(rights, rpart, src * rrows, axis=1)

    zlo_size = shards // Y_SIZE
    nz = groups * zlo_size
    zi = gi * zlo_size + si // Y_SIZE
    n_all = groups * shards * tensors

    def zshift(k):
        pairs = []
        for i in range(n_all):
            gs, t = i // tensors, i % tensors
            z, y = gs // Y_SIZE, gs % Y_SIZE
            d = k if t % 2 == 0 else -k
            pairs.append((i, (((z + d) % nz) * Y_SIZE + y) * tensors + t))
        return pairs

    out = jnp.zeros((nz,) + yblk.shape, piece.dtype)
    out = lax.dynamic_update_index_in_dim(out, yblk, zi, axis=0)
    half = nz // 2
    reach = half // 2
    rel = jnp.zeros((2 * reach + 1,) + yblk.shape, piece.dtype)
    rel = lax.dynamic_update_index_in_dim(rel, yblk, reach, axis=0)
    fwd = yblk
    bwd = yblk
    axes = ("group", "shard", "tensor")
    for step in range(1, reach + 1):
        fwd = lax.ppermute(fwd, axes, zshift(2))
        j = -step * sgn
        out = lax.dynamic_update_index_in_dim(out, fwd, (zi + 2 * j) % nz, axis=0)
        if step < reach:
            rel = lax.dynamic_update_index_in_dim(rel, fwd, j + reach, axis=0)
        if step < half - reach:
            bwd = lax.ppermute(bwd, axes, zshift(-2))
            out = lax.dynamic_update_index_in_dim(out, bwd, (zi - 2 * j) % nz, axis=0)
            rel = lax.dynamic_update_index_in_dim(rel, bwd, reach - j, axis=0)
    nsend = reach
    up_start = reach
    down_start = reach - (nsend - 1)
    for k, first in ((-1, (up_start + down_start + (up_start - down_start) * sgn) // 2),
                     (1, (up_start + down_start - (up_start - down_start) * sgn) // 2)):
        part = lax.dynamic_slice_in_dim(rel, first, nsend, axis=0)
        got = lax.ppermute(part, axes, zshift(k))
        src_z = zi - k * sgn
        for m in range(nsend):
            zabs = (src_z + 2 * (first - reach + m)) % nz
            out = lax.dynamic_update_index_in_dim(out, got[m], zabs, axis=0)
    layer_blocks = jnp.moveaxis(out, 2, 0).reshape(piece.shape[0], -1, piece.shape[2])

    lefts = received(nlayer, nleft).reshape((groups,) + left.shape[1:])
    total = jnp.zeros(emb_weight.shape, f32)
    for g in range(groups):
        product = jnp.dot(lefts[g], rights[g], preferred_element_type=f32).astype(bf16)
        total = total + product.astype(f32)
    emb_mean = total / groups
    new_emb_momentum = beta_outer * emb_momentum + emb_mean
    new_emb_weight = emb_weight - rate_outer * (emb_mean + beta_outer * new_emb_momentum)
    return (new_layer_weight, new_layer_momentum, layer_blocks, new_emb_weight, new_emb_momentum)


def solution(mesh):
    placed = (
        P("group", None, None, "shard", "tensor"),
        P("group", None, ("shard", "tensor"), None),
        P("group", None, None),
        P(None, ("group", "shard"), "tensor"),
        P(None, ("group", "shard"), "tensor"),
        P(("group", "shard", "tensor"), None),
        P(("group", "shard", "tensor"), None),
    )
    return jax.shard_map(
        on_device,
        mesh=mesh,
        in_specs=placed,
        out_specs=(
            P(None, ("group", "shard"), "tensor"),
            P(None, ("group", "shard"), "tensor"),
            P(None, None, "tensor"),
            P(("group", "shard", "tensor"), None),
            P(("group", "shard", "tensor"), None),
        ),
        check_vma=False,
    )
```

```python
import jax
import jax.numpy as jnp
from jax import lax
from jax.sharding import PartitionSpec as P

rate_outer = 0.7
beta_outer = 0.9

Y_SIZE = 4


def shift_pairs(n, k):
    return [(i, (i + k) % n) for i in range(n)]


def on_device(
    layer_delta, emb_left, emb_right, layer_weight, layer_momentum, emb_weight, emb_momentum
):
    f32 = jnp.float32
    bf16 = jnp.bfloat16
    groups = lax.axis_size("group")
    shards = lax.axis_size("shard")
    tensors = lax.axis_size("tensor")
    gi = lax.axis_index("group")
    si = lax.axis_index("shard")
    ti = lax.axis_index("tensor")

    delta = layer_delta[0]
    nlayer = delta.size // groups
    send_layer = jnp.moveaxis(delta, 1, 0).reshape(groups, nlayer)
    left = emb_left[0]
    nleft = left.size // groups
    send_left = left.reshape(groups, nleft)
    right = emb_right[0]
    rank, width = right.shape
    rrows = rank // Y_SIZE
    ry = lax.dynamic_slice_in_dim(right, (si % Y_SIZE) * rrows, rrows, axis=0)
    send_right = jnp.broadcast_to(ry.reshape(1, rrows * width), (groups, rrows * width))
    parts = [send_layer, send_left, send_right]
    send = jnp.concatenate([p.reshape(groups, 2, p.shape[1] // 2) for p in parts], axis=2)
    recv_halves = lax.all_to_all(send, "group", 0, 0, tiled=True)

    def received(offset, n):
        return recv_halves[:, :, offset // 2:(offset + n) // 2].reshape(groups, n)

    acc = received(0, nlayer).astype(f32).sum(axis=0)
    layer_mean = acc.reshape(layer_weight.shape) / groups
    new_layer_momentum = beta_outer * layer_momentum + layer_mean
    new_layer_weight = layer_weight - rate_outer * (layer_mean + beta_outer * new_layer_momentum)
    piece = new_layer_weight.astype(bf16)

    sgn = 1 - 2 * (ti % 2)
    n_st = shards * tensors

    def yshift(k):
        pairs = []
        for i in range(n_st):
            s, t = i // tensors, i % tensors
            d = k if t % 2 == 0 else -k
            pairs.append((i, ((s - s % Y_SIZE) + (s % Y_SIZE + d) % Y_SIZE) * tensors + t))
        return pairs

    yi = si % Y_SIZE
    rgot = received(nlayer + nleft, rrows * width)
    npiece = piece.size
    payload = jnp.concatenate([piece.reshape(2, npiece // 2), rgot.reshape(2, -1)], axis=1)
    yblk = jnp.zeros((Y_SIZE,) + piece.shape, piece.dtype)
    yblk = lax.dynamic_update_index_in_dim(yblk, piece, yi, axis=0)
    rights = jnp.zeros((groups, rank, width), rgot.dtype)
    rights = lax.dynamic_update_slice_in_dim(rights, rgot.reshape(groups, rrows, width), yi * rrows, axis=1)
    for k in (1, -1, 2):
        got = lax.ppermute(payload, ("shard", "tensor"), yshift(k))
        src = (yi - k * sgn) % Y_SIZE
        yblk = lax.dynamic_update_index_in_dim(yblk, got[:, :npiece // 2].reshape(piece.shape), src, axis=0)
        rpart = got[:, npiece // 2:].reshape(groups, rrows, width)
        rights = lax.dynamic_update_slice_in_dim(rights, rpart, src * rrows, axis=1)

    zlo_size = shards // Y_SIZE
    nz = groups * zlo_size
    zi = gi * zlo_size + si // Y_SIZE
    n_all = groups * shards * tensors

    def zshift(k):
        pairs = []
        for i in range(n_all):
            gs, t = i // tensors, i % tensors
            z, y = gs // Y_SIZE, gs % Y_SIZE
            d = k if t % 2 == 0 else -k
            pairs.append((i, (((z + d) % nz) * Y_SIZE + y) * tensors + t))
        return pairs

    out = jnp.zeros((nz,) + yblk.shape, piece.dtype)
    out = lax.dynamic_update_index_in_dim(out, yblk, zi, axis=0)
    half = nz // 2
    reach = half // 2
    rel = jnp.zeros((2 * reach + 1,) + yblk.shape, piece.dtype)
    rel = lax.dynamic_update_index_in_dim(rel, yblk, reach, axis=0)
    fwd = yblk
    bwd = yblk
    axes = ("group", "shard", "tensor")
    for step in range(1, reach + 1):
        fwd = lax.ppermute(fwd, axes, zshift(2))
        j = -step * sgn
        out = lax.dynamic_update_index_in_dim(out, fwd, (zi + 2 * j) % nz, axis=0)
        if step < reach:
            rel = lax.dynamic_update_index_in_dim(rel, fwd, j + reach, axis=0)
        if step < half - reach:
            bwd = lax.ppermute(bwd, axes, zshift(-2))
            out = lax.dynamic_update_index_in_dim(out, bwd, (zi - 2 * j) % nz, axis=0)
            rel = lax.dynamic_update_index_in_dim(rel, bwd, reach - j, axis=0)
    nsend = reach
    up_start = reach
    down_start = reach - (nsend - 1)
    for k, first in ((-1, (up_start + down_start + (up_start - down_start) * sgn) // 2),
                     (1, (up_start + down_start - (up_start - down_start) * sgn) // 2)):
        part = lax.dynamic_slice_in_dim(rel, first, nsend, axis=0)
        got = lax.ppermute(part, axes, zshift(k))
        src_z = zi - k * sgn
        for m in range(nsend):
            zabs = (src_z + 2 * (first - reach + m)) % nz
            out = lax.dynamic_update_index_in_dim(out, got[m], zabs, axis=0)
    layer_blocks = jnp.moveaxis(out, 2, 0).reshape(piece.shape[0], -1, piece.shape[2])

    lefts = received(nlayer, nleft).reshape((groups,) + left.shape[1:])
    total = jnp.zeros(emb_weight.shape, f32)
    for g in range(groups):
        product = jnp.dot(lefts[g], rights[g], preferred_element_type=f32).astype(bf16)
        total = total + product.astype(f32)
    emb_mean = total / groups
    new_emb_momentum = beta_outer * emb_momentum + emb_mean
    new_emb_weight = emb_weight - rate_outer * (emb_mean + beta_outer * new_emb_momentum)
    return (new_layer_weight, new_layer_momentum, layer_blocks, new_emb_weight, new_emb_momentum)


def solution(mesh):
    placed = (
        P("group", None, None, "shard", "tensor"),
        P("group", None, ("shard", "tensor"), None),
        P("group", None, None),
        P(None, ("group", "shard"), "tensor"),
        P(None, ("group", "shard"), "tensor"),
        P(("group", "shard", "tensor"), None),
        P(("group", "shard", "tensor"), None),
    )
    return jax.shard_map(
        on_device,
        mesh=mesh,
        in_specs=placed,
        out_specs=(
            P(None, ("group", "shard"), "tensor"),
            P(None, ("group", "shard"), "tensor"),
            P(None, None, "tensor"),
            P(("group", "shard", "tensor"), None),
            P(("group", "shard", "tensor"), None),
        ),
        check_vma=False,
    )
```

```python
import jax
import jax.numpy as jnp
from jax import lax
from jax.sharding import PartitionSpec as P

rate_outer = 0.7
beta_outer = 0.9

Y_SIZE = 4


def shift_pairs(n, k):
    return [(i, (i + k) % n) for i in range(n)]


def on_device(
    layer_delta, emb_left, emb_right, layer_weight, layer_momentum, emb_weight, emb_momentum
):
    f32 = jnp.float32
    bf16 = jnp.bfloat16
    groups = lax.axis_size("group")
    shards = lax.axis_size("shard")
    tensors = lax.axis_size("tensor")
    gi = lax.axis_index("group")
    si = lax.axis_index("shard")
    ti = lax.axis_index("tensor")

    delta = layer_delta[0]
    nlayer = delta.size // groups
    send_layer = jnp.moveaxis(delta, 1, 0).reshape(groups, nlayer)
    left = emb_left[0]
    nleft = left.size // groups
    send_left = left.reshape(groups, nleft)
    right = emb_right[0]
    rank, width = right.shape
    rrows = rank // Y_SIZE
    ry = lax.dynamic_slice_in_dim(right, (si % Y_SIZE) * rrows, rrows, axis=0)
    send_right = jnp.broadcast_to(ry.reshape(1, rrows * width), (groups, rrows * width))
    parts = [send_layer, send_left, send_right]
    send = jnp.concatenate([p.reshape(groups, 2, p.shape[1] // 2) for p in parts], axis=2)
    recv_halves = lax.all_to_all(send, "group", 0, 0, tiled=True)

    def received(offset, n):
        return recv_halves[:, :, offset // 2:(offset + n) // 2].reshape(groups, n)

    acc = received(0, nlayer).astype(f32).sum(axis=0)
    layer_mean = acc.reshape(layer_weight.shape) / groups
    new_layer_momentum = beta_outer * layer_momentum + layer_mean
    new_layer_weight = layer_weight - rate_outer * (layer_mean + beta_outer * new_layer_momentum)
    piece = new_layer_weight.astype(bf16)

    sgn = 1 - 2 * (ti % 2)
    n_st = shards * tensors

    def yshift(k):
        pairs = []
        for i in range(n_st):
            s, t = i // tensors, i % tensors
            d = k if t % 2 == 0 else -k
            pairs.append((i, ((s - s % Y_SIZE) + (s % Y_SIZE + d) % Y_SIZE) * tensors + t))
        return pairs

    yi = si % Y_SIZE
    rgot = received(nlayer + nleft, rrows * width)
    npiece = piece.size
    payload = jnp.concatenate([piece.reshape(2, npiece // 2), rgot.reshape(2, -1)], axis=1)
    yblk = jnp.zeros((Y_SIZE,) + piece.shape, piece.dtype)
    yblk = lax.dynamic_update_index_in_dim(yblk, piece, yi, axis=0)
    rights = jnp.zeros((groups, rank, width), rgot.dtype)
    rights = lax.dynamic_update_slice_in_dim(rights, rgot.reshape(groups, rrows, width), yi * rrows, axis=1)
    for k in (1, -1, 2):
        got = lax.ppermute(payload, ("shard", "tensor"), yshift(k))
        src = (yi - k * sgn) % Y_SIZE
        yblk = lax.dynamic_update_index_in_dim(yblk, got[:, :npiece // 2].reshape(piece.shape), src, axis=0)
        rpart = got[:, npiece // 2:].reshape(groups, rrows, width)
        rights = lax.dynamic_update_slice_in_dim(rights, rpart, src * rrows, axis=1)

    zlo_size = shards // Y_SIZE
    nz = groups * zlo_size
    zi = gi * zlo_size + si // Y_SIZE
    n_all = groups * shards * tensors

    def zshift(k):
        pairs = []
        for i in range(n_all):
            gs, t = i // tensors, i % tensors
            z, y = gs // Y_SIZE, gs % Y_SIZE
            d = k if t % 2 == 0 else -k
            pairs.append((i, (((z + d) % nz) * Y_SIZE + y) * tensors + t))
        return pairs

    out = jnp.zeros((nz,) + yblk.shape, piece.dtype)
    out = lax.dynamic_update_index_in_dim(out, yblk, zi, axis=0)
    half = nz // 2
    reach = half // 2
    rel = jnp.zeros((2 * reach + 1,) + yblk.shape, piece.dtype)
    rel = lax.dynamic_update_index_in_dim(rel, yblk, reach, axis=0)
    fwd = yblk
    bwd = yblk
    axes = ("group", "shard", "tensor")
    for step in range(1, reach + 1):
        fwd = lax.ppermute(fwd, axes, zshift(2))
        j = -step * sgn
        out = lax.dynamic_update_index_in_dim(out, fwd, (zi + 2 * j) % nz, axis=0)
        if step < reach:
            rel = lax.dynamic_update_index_in_dim(rel, fwd, j + reach, axis=0)
        if step < half - reach:
            bwd = lax.ppermute(bwd, axes, zshift(-2))
            out = lax.dynamic_update_index_in_dim(out, bwd, (zi - 2 * j) % nz, axis=0)
            rel = lax.dynamic_update_index_in_dim(rel, bwd, reach - j, axis=0)
    nsend = reach
    up_start = reach
    down_start = reach - (nsend - 1)
    for k, first in ((-1, (up_start + down_start + (up_start - down_start) * sgn) // 2),
                     (1, (up_start + down_start - (up_start - down_start) * sgn) // 2)):
        part = lax.dynamic_slice_in_dim(rel, first, nsend, axis=0)
        got = lax.ppermute(part, axes, zshift(k))
        src_z = zi - k * sgn
        for m in range(nsend):
            zabs = (src_z + 2 * (first - reach + m)) % nz
            out = lax.dynamic_update_index_in_dim(out, got[m], zabs, axis=0)
    layer_blocks = jnp.moveaxis(out, 2, 0).reshape(piece.shape[0], -1, piece.shape[2])

    lefts = received(nlayer, nleft).reshape((groups,) + left.shape[1:])
    products = jnp.einsum("gvr,grd->gvd", lefts, rights, preferred_element_type=f32).astype(bf16)
    total = products[0].astype(f32)
    for g in range(1, groups):
        total = total + products[g].astype(f32)
    emb_mean = total / groups
    new_emb_momentum = beta_outer * emb_momentum + emb_mean
    new_emb_weight = emb_weight - rate_outer * (emb_mean + beta_outer * new_emb_momentum)
    return (new_layer_weight, new_layer_momentum, layer_blocks, new_emb_weight, new_emb_momentum)


def solution(mesh):
    placed = (
        P("group", None, None, "shard", "tensor"),
        P("group", None, ("shard", "tensor"), None),
        P("group", None, None),
        P(None, ("group", "shard"), "tensor"),
        P(None, ("group", "shard"), "tensor"),
        P(("group", "shard", "tensor"), None),
        P(("group", "shard", "tensor"), None),
    )
    return jax.shard_map(
        on_device,
        mesh=mesh,
        in_specs=placed,
        out_specs=(
            P(None, ("group", "shard"), "tensor"),
            P(None, ("group", "shard"), "tensor"),
            P(None, None, "tensor"),
            P(("group", "shard", "tensor"), None),
            P(("group", "shard", "tensor"), None),
        ),
        check_vma=False,
    )
```
